1024 devices in a mesh: dp: 4 (over x), expert: 32 (over z, core), tensor: 8 (over y).
Axes of the slice: x: 4, y: 8, z: 16, core: 2. Of those that a mesh axis runs over, the one named last changes fastest.
Arguments:
- tokens: bfloat16 [8192, 4096], P(('dp', 'expert'), 'tensor'), may hold values from -6 to 6
- expert_ids: int32 [8192, 8], P(('dp', 'expert')), may hold values from 0 to 63, all different within a row; in each aligned block of 64 rows (0 to 63, 64 to 127, ...) at most 9 rows name the same one
- combine_weight: float32 [8192, 8], P(('dp', 'expert')), may hold values from 0.05 to 0.4
- w_gate: bfloat16 [64, 4096, 1536], P('expert', None, 'tensor'), may hold values from -0.09375 to 0.09375
- w_up: bfloat16 [64, 4096, 1536], P('expert', None, 'tensor'), may hold values from -0.09375 to 0.09375
- w_down: bfloat16 [64, 1536, 4096], P('expert', 'tensor'), may hold values from -0.15625 to 0.15625
Outputs:
- mixed: bfloat16 [8192, 4096], P(('dp', 'expert'), 'tensor')
- expert_load: float32 [64], replicated
The draws below stay inside these ranges and needn't reach their ends.
Inputs may be any that keep to these rules, and one draw needn't show every extreme that they name: `expert_ids`: each row names 8 different experts. In the rows of one token group no expert is named by more than 9 rows, and that most is reached.
All inputs are finite; a program needn't handle non-finite values.
Results may differ from the reference program's by a relative error of at most 0.015.
Values may be sent and summed in bfloat16 or wider, within the bound.
No kernel may reach another device: no remote copies, remote signals or barrier semaphores. Data moves between devices by JAX's collectives and lax.ppermute only.
A program may use at most 64 MiB of HBM per device.

```python
import math
import jax
import jax.numpy as jnp
import numpy as np
from jax import lax

D = 4096
HID = 1536
TOPK = 8
TOK_DEV = 64
EXPERTS = 64
CAP = 9
TOKENS = 8192
N_DP = 4
N_EXPERT = 32
N_TENSOR = 8


def levels(stream_key, shape, cuts, smallest, largest):
    loudness = 1.0
    for dim, blocks in cuts:
        heights = jax.random.uniform(jax.random.fold_in(jax.random.fold_in(stream_key, 6), dim), (blocks,), jnp.float32, smallest / len(cuts), largest / len(cuts))
        loudness = loudness * jnp.repeat(jnp.exp(heights), shape[dim] // blocks).reshape((-1,) + (1,) * (len(shape) - 1 - dim))
    return loudness


def deal_out(own_key, own, number, rows, count, top, reach, lean):
    order = jax.random.permutation(own_key, count)
    crowded, usual = portions_of(count, rows * top, reach, lean, True), portions_of(count, rows * top, reach, lean, False)
    places = jnp.arange(count)

    def named(tallies, offset_by):
        used = int((tallies > 0).sum())
        fixed = max(1, used // 4)
        moved = fixed + (places - fixed + offset_by * (used - fixed)) % max(1, count - fixed)
        return jnp.zeros((count,), jnp.int32).at[order[jnp.where(places < fixed, places, moved)]].set(jnp.asarray(tallies, jnp.int32))

    tallies = jnp.where(number % 4 == 0, named(crowded, number // 4), named(usual, number - number // 4 - 1))
    mixed = jax.random.permutation(jax.random.fold_in(own, 3), count)
    source_of, sink = mixed[0:count // 2 * 2:2], mixed[1:count // 2 * 2:2]
    margin = jnp.minimum(tallies[source_of] - 1, reach - tallies[sink]) // 2
    margin = jnp.where((source_of == order[0]) | (sink == order[0]) | (tallies[sink] == 0), 0, jnp.maximum(margin, 0))
    moved = jax.random.randint(jax.random.fold_in(own, 4), (count // 2,), 0, 1 << 20) % (margin + 1)
    tallies = tallies.at[source_of].add(-moved).at[sink].add(moved)
    members = jnp.searchsorted(jnp.cumsum(tallies), jnp.arange(rows * top), side="right").astype(jnp.int32)
    table = members.reshape(top, rows).T
    table = table[jax.random.permutation(jax.random.fold_in(own, 1), rows)]
    offset_by = jax.random.randint(jax.random.fold_in(own, 2), (rows, 1), 0, top)
    return jnp.take_along_axis(table, (jnp.arange(top)[None, :] + offset_by) % top, axis=1)


def portions_of(count, total, bound, slope, full):
    loads = [(1 << 20) // math.isqrt(standing ** slope) + 1 for standing in range(1, count + 1)]
    largest = bound if full else min(bound, max(-(-total // count), total * loads[0] // sum(loads)))
    least = 1 if total - largest >= count - 1 else 0
    counts, rest = [largest] + [least] * (count - 1), total - largest - least * (count - 1)
    while rest > 0:
        candidates = [i for i in range(1, count) if counts[i] < largest] or [i for i in range(1, count) if counts[i] < bound]
        whole, remaining = sum([loads[i] for i in candidates]), rest
        for i in candidates:
            extra = min(bound - counts[i], max(1, remaining * loads[i] // whole), rest)
            counts[i] = counts[i] + extra
            rest = rest - extra
    return np.array(counts)


def noise(rng, extent, deviation, bound, cuts=(), held_as=jnp.bfloat16):
    gain = levels(rng, extent, cuts, -0.22, 0.18) if cuts else 1.0
    result = jax.random.normal(rng, extent, jnp.float32) * deviation * gain
    return jnp.minimum(jnp.maximum(result, -bound), bound).astype(held_as)


def setup_inputs(seed: int = 0) -> dict:
    key_list = jax.random.split(jax.random.key(seed), 7)
    tokens = noise(key_list[0], (TOKENS, D), 1.0, 6.0, ((0, 128), (1, 8)))
    expert_ids_keys = jax.random.split(jax.random.fold_in(key_list[1], 1), TOKENS // TOK_DEV)
    expert_ids_turns = jax.random.permutation(jax.random.fold_in(key_list[1], 3), TOKENS // TOK_DEV)
    expert_ids = jax.vmap(lambda own, number: deal_out(jax.random.fold_in(key_list[1], 2), own, number, TOK_DEV, EXPERTS, TOPK, CAP, 2))(expert_ids_keys, expert_ids_turns).reshape((TOKENS, TOPK))
    combine_weight = jnp.clip(jnp.exp(math.log(0.4) - 2.0794415 * jax.random.uniform(key_list[2], (TOKENS, TOPK), jnp.float32) ** levels(key_list[2], (TOKENS, TOPK), ((0, 128),), -0.2, 0.2)), 0.05, 0.4)
    w_gate = noise(key_list[3], (EXPERTS, D, HID), D ** -0.5, 0.09375, ((0, 32), (2, 8)))
    w_up = noise(key_list[4], (EXPERTS, D, HID), D ** -0.5, 0.09375, ((0, 32), (2, 8)))
    w_down = noise(key_list[5], (EXPERTS, HID, D), HID ** -0.5, 0.15625, ((0, 32), (1, 8)))
    return {"tokens": tokens, "expert_ids": expert_ids, "combine_weight": combine_weight, "w_gate": w_gate, "w_up": w_up, "w_down": w_down}


def slots_of(ids):
    onehot = (ids[:, None] == jnp.arange(EXPERTS, dtype=jnp.int32)[None, :]).astype(jnp.int32)
    return jnp.sum((jnp.cumsum(onehot, axis=0) - onehot) * onehot, axis=1).astype(jnp.int32)


def reference(tokens, expert_ids, combine_weight, w_gate, w_up, w_down):
    groups = N_DP * N_EXPERT
    pairs = TOK_DEV * TOPK
    width = HID // N_TENSOR
    ids_grouped = expert_ids.reshape(groups, pairs)
    ranks = jax.vmap(slots_of)(ids_grouped)
    group_index = jnp.arange(groups, dtype=jnp.int32)[:, None]
    position = ids_grouped * (groups * CAP) + group_index * CAP + ranks
    token_of = group_index * TOK_DEV + jnp.arange(pairs, dtype=jnp.int32)[None, :] // TOPK
    table = jnp.full((EXPERTS * groups * CAP,), -1, jnp.int32).at[position.reshape(-1)].set(token_of.reshape(-1))

    def one_expert(index):
        picked = lax.dynamic_slice_in_dim(table, (index * groups * CAP).astype(jnp.int32), groups * CAP)
        rows = jnp.where((picked >= 0)[:, None], tokens[jnp.maximum(picked, 0)], jnp.zeros((), jnp.bfloat16))
        gate = jnp.dot(rows, w_gate[index], preferred_element_type=jnp.float32)
        up = jnp.dot(rows, w_up[index], preferred_element_type=jnp.float32)
        hidden = (jax.nn.silu(gate) * up).astype(jnp.bfloat16)
        hidden_blocks = hidden.astype(jnp.float32).reshape(groups * CAP, N_TENSOR, width)
        down_blocks = w_down[index].astype(jnp.float32).reshape(N_TENSOR, width, D)
        parts = jnp.einsum("rth,thd->trd", hidden_blocks, down_blocks).astype(jnp.bfloat16)
        parts = lax.optimization_barrier(parts)
        return jnp.sum(parts.astype(jnp.float32), axis=0).astype(jnp.bfloat16)

    outputs = lax.map(one_expert, jnp.arange(EXPERTS, dtype=jnp.int32))
    flat_out = outputs.reshape(EXPERTS * groups * CAP, D)
    where_pair = position.reshape(TOKENS, TOPK)
    total = jnp.zeros((TOKENS, D), jnp.float32)
    for k in range(TOPK):
        total = total + combine_weight[:, k:k + 1] * flat_out[where_pair[:, k]].astype(jnp.float32)
    mixed = total.astype(jnp.bfloat16)
    summed = jax.ops.segment_sum(combine_weight.reshape(-1), expert_ids.reshape(-1), num_segments=EXPERTS)
    expert_load = (summed * (EXPERTS / TOKENS)).astype(jnp.float32)
    return mixed, expert_load
```

```python
import jax
import jax.numpy as jnp
from jax import lax
from jax.sharding import PartitionSpec as P


def on_device(tokens, expert_ids, combine_weight, w_gate, w_up, w_down):
    owners = lax.axis_size("expert")
    splits = lax.axis_size("tensor")
    local = w_gate.shape[0]
    experts = owners * local
    tok_rows = tokens.shape[0]
    chosen = expert_ids.shape[1]
    capacity = min(tok_rows, (9 * tok_rows * chosen + 8 * experts - 1) // (8 * experts))
    flat_ids = expert_ids.reshape(-1)
    onehot = (flat_ids[:, None] == jnp.arange(experts, dtype=jnp.int32)[None, :]).astype(jnp.int32)
    ranks = jnp.sum((jnp.cumsum(onehot, axis=0) - onehot) * onehot, axis=1)
    target = flat_ids * capacity + ranks
    pair_count = flat_ids.shape[0]
    source = (
        jnp.full((experts * capacity,), -1, jnp.int32)
        .at[target]
        .set(jnp.arange(pair_count, dtype=jnp.int32) // chosen)
    )
    filled = (source >= 0)[:, None]
    safe = jnp.maximum(source, 0)
    outgoing = jnp.where(filled, tokens[safe], jnp.zeros((), jnp.bfloat16))
    outgoing = outgoing.reshape(owners, local * capacity, tokens.shape[1])
    sliced = lax.all_to_all(outgoing, "expert", split_axis=0, concat_axis=0, tiled=True)
    arrived = lax.all_gather(sliced, "tensor", axis=2, tiled=True)
    model_width = arrived.shape[2]
    stacked = arrived.reshape(owners, local, capacity, model_width)
    rows = jnp.transpose(stacked, (1, 0, 2, 3)).reshape(local, owners * capacity, model_width)
    gate = jnp.einsum("erd,edh->erh", rows, w_gate, preferred_element_type=jnp.float32)
    up = jnp.einsum("erd,edh->erh", rows, w_up, preferred_element_type=jnp.float32)
    hidden = (jax.nn.silu(gate) * up).astype(jnp.bfloat16)
    feature_cols = model_width // splits
    summed_out = lax.psum_scatter(
        jnp.einsum("erh,ehd->der", hidden, w_down, preferred_element_type=jnp.float32).astype(
            jnp.bfloat16
        ),
        "tensor",
        scatter_dimension=0,
        tiled=True,
    )
    expert_out = jnp.transpose(
        summed_out.reshape(feature_cols, local, owners, capacity), (2, 1, 3, 0)
    )
    expert_out = expert_out.reshape(owners, local * capacity, feature_cols)
    back = lax.all_to_all(expert_out, "expert", split_axis=0, concat_axis=0, tiled=True)
    back = back.reshape(experts * capacity, feature_cols)
    picked = back[target].astype(jnp.float32)
    weighted = picked * combine_weight.reshape(-1)[:, None]
    mixed = jnp.sum(weighted.reshape(tok_rows, chosen, feature_cols), axis=1).astype(jnp.bfloat16)
    group_load = jnp.sum(onehot.astype(jnp.float32) * combine_weight.reshape(-1)[:, None], axis=0)
    row_load = jnp.sum(lax.all_gather(group_load, "expert", axis=0), axis=0)
    total_load = jnp.sum(lax.all_gather(row_load, "dp", axis=0), axis=0)
    all_tokens = tok_rows * lax.axis_size("dp") * owners
    expert_load = total_load * (experts / all_tokens)
    return (mixed, expert_load)


def solution(mesh):
    in_specs = (
        P(("dp", "expert"), "tensor"),
        P(("dp", "expert"), None),
        P(("dp", "expert"), None),
        P("expert", None, "tensor"),
        P("expert", None, "tensor"),
        P("expert", "tensor", None),
    )
    out_specs = (P(("dp", "expert"), "tensor"), P())
    return jax.shard_map(
        on_device, mesh=mesh, in_specs=in_specs, out_specs=out_specs, check_vma=False
    )
```

```python
import jax
import jax.numpy as jnp
from jax import lax
from jax.sharding import PartitionSpec as P


def on_device(tokens, expert_ids, combine_weight, w_gate, w_up, w_down):
    owners = lax.axis_size("expert")
    local = w_gate.shape[0]
    experts = owners * local
    tok_rows, feature_cols = tokens.shape
    chosen = expert_ids.shape[1]
    capacity = min(tok_rows, (9 * tok_rows * chosen + 8 * experts - 1) // (8 * experts))
    flat_ids = expert_ids.reshape(-1)
    onehot = (flat_ids[:, None] == jnp.arange(experts, dtype=jnp.int32)[None, :]).astype(jnp.int32)
    ranks = jnp.sum((jnp.cumsum(onehot, axis=0) - onehot) * onehot, axis=1)
    target = flat_ids * capacity + ranks
    pair_count = flat_ids.shape[0]
    source = (
        jnp.full((experts * capacity,), -1, jnp.int32)
        .at[target]
        .set(jnp.arange(pair_count, dtype=jnp.int32) // chosen)
    )
    filled = (source >= 0)[:, None]
    safe = jnp.maximum(source, 0)
    outgoing = jnp.where(filled, tokens[safe], jnp.zeros((), jnp.bfloat16))
    outgoing = outgoing.reshape(owners, local, capacity, feature_cols)
    group_load = jnp.sum(onehot.astype(jnp.float32) * combine_weight.reshape(-1)[:, None], axis=0)
    load_row = jnp.zeros((owners, 1, feature_cols), jnp.bfloat16)
    load_row = load_row.at[:, 0, :local].set(group_load.reshape(owners, local).astype(jnp.bfloat16))

    pieces = []
    owner_part = None
    total_load = None
    for c in range(local):
        send = outgoing[:, c]
        if c == 0:
            send = jnp.concatenate([send, load_row], axis=1)
        got = lax.all_to_all(send, "expert", split_axis=0, concat_axis=0, tiled=True)
        if c == 0:
            owner_part = jnp.sum(got[:, capacity, :local].astype(jnp.float32), axis=0)
            got = got[:, :capacity]
        arrived = lax.all_gather(got, "tensor", axis=2, tiled=True)
        model_width = arrived.shape[2]
        rows = arrived.reshape(owners * capacity, model_width)
        gate = jnp.dot(rows, w_gate[c], preferred_element_type=jnp.float32)
        up = jnp.dot(rows, w_up[c], preferred_element_type=jnp.float32)
        hidden = (jax.nn.silu(gate) * up).astype(jnp.bfloat16)
        down = jnp.einsum(
            "rh,hd->dr", hidden, w_down[c], preferred_element_type=jnp.float32
        ).astype(jnp.bfloat16)
        summed = lax.psum_scatter(down, "tensor", scatter_dimension=0, tiled=True)
        back_send = jnp.transpose(summed.reshape(feature_cols, owners, capacity), (1, 2, 0))
        if c == local - 1:
            owner_total = lax.psum(owner_part, "dp")
            total_row = jnp.zeros((owners, 1, feature_cols), jnp.bfloat16)
            total_row = total_row.at[:, 0, :local].set(
                jnp.broadcast_to(owner_total.astype(jnp.bfloat16)[None, :], (owners, local))
            )
            back_send = jnp.concatenate([back_send, total_row], axis=1)
        back = lax.all_to_all(back_send, "expert", split_axis=0, concat_axis=0, tiled=True)
        if c == local - 1:
            total_load = back[:, capacity, :local].astype(jnp.float32).reshape(experts)
            back = back[:, :capacity]
        pieces.append(back)
    back = jnp.stack(pieces, axis=1).reshape(experts * capacity, feature_cols)
    picked = back[target].astype(jnp.float32)
    weighted = picked * combine_weight.reshape(-1)[:, None]
    mixed = jnp.sum(weighted.reshape(tok_rows, chosen, feature_cols), axis=1).astype(jnp.bfloat16)
    all_tokens = tok_rows * lax.axis_size("dp") * owners
    expert_load = total_load * (experts / all_tokens)
    return (mixed, expert_load)


def solution(mesh):
    in_specs = (
        P(("dp", "expert"), "tensor"),
        P(("dp", "expert"), None),
        P(("dp", "expert"), None),
        P("expert", None, "tensor"),
        P("expert", None, "tensor"),
        P("expert", "tensor", None),
    )
    out_specs = (P(("dp", "expert"), "tensor"), P())
    return jax.shard_map(
        on_device, mesh=mesh, in_specs=in_specs, out_specs=out_specs, check_vma=False
    )
```

```python
import jax
import jax.numpy as jnp
from jax import lax
from jax.sharding import PartitionSpec as P


def on_device(tokens, expert_ids, combine_weight, w_gate, w_up, w_down):
    owners = lax.axis_size("expert")
    local = w_gate.shape[0]
    experts = owners * local
    tok_rows, feature_cols = tokens.shape
    chosen = expert_ids.shape[1]
    capacity = min(tok_rows, (9 * tok_rows * chosen + 8 * experts - 1) // (8 * experts))
    flat_ids = expert_ids.reshape(-1)
    onehot = (flat_ids[:, None] == jnp.arange(experts, dtype=jnp.int32)[None, :]).astype(jnp.int32)
    ranks = jnp.sum((jnp.cumsum(onehot, axis=0) - onehot) * onehot, axis=1)
    target = flat_ids * capacity + ranks
    pair_count = flat_ids.shape[0]
    source = (
        jnp.full((experts * capacity,), -1, jnp.int32)
        .at[target]
        .set(jnp.arange(pair_count, dtype=jnp.int32) // chosen)
    )
    filled = (source >= 0)[:, None]
    safe = jnp.maximum(source, 0)
    outgoing = jnp.where(filled, tokens[safe], jnp.zeros((), jnp.bfloat16))
    outgoing = outgoing.reshape(owners, local, capacity, feature_cols)
    group_load = jnp.sum(onehot.astype(jnp.float32) * combine_weight.reshape(-1)[:, None], axis=0)
    load_row = jnp.zeros((owners, 1, feature_cols), jnp.bfloat16)
    load_row = load_row.at[:, 0, :local].set(group_load.reshape(owners, local).astype(jnp.bfloat16))

    send = jnp.concatenate(
        [outgoing.reshape(owners, local * capacity, feature_cols), load_row], axis=1
    )
    got = lax.all_to_all(send, "expert", split_axis=0, concat_axis=0, tiled=True)
    owner_part = jnp.sum(got[:, local * capacity, :local].astype(jnp.float32), axis=0)
    got = got[:, : local * capacity].reshape(owners, local, capacity, feature_cols)
    got = jnp.transpose(got, (1, 0, 2, 3)).reshape(local * owners * capacity, feature_cols)
    arrived = lax.all_gather(got, "tensor", axis=1, tiled=True)
    model_width = arrived.shape[1]
    rows = arrived.reshape(local, owners * capacity, model_width)
    gate = jnp.einsum("erd,edh->erh", rows, w_gate, preferred_element_type=jnp.float32)
    up = jnp.einsum("erd,edh->erh", rows, w_up, preferred_element_type=jnp.float32)
    hidden = (jax.nn.silu(gate) * up).astype(jnp.bfloat16)
    down = jnp.einsum("erh,ehd->der", hidden, w_down, preferred_element_type=jnp.float32).astype(
        jnp.bfloat16
    )
    summed = lax.psum_scatter(down, "tensor", scatter_dimension=0, tiled=True)
    back_send = jnp.transpose(
        summed.reshape(feature_cols, local, owners, capacity), (2, 1, 3, 0)
    ).reshape(owners, local * capacity, feature_cols)
    owner_total = lax.psum(owner_part, "dp")
    total_row = jnp.zeros((owners, 1, feature_cols), jnp.bfloat16)
    total_row = total_row.at[:, 0, :local].set(
        jnp.broadcast_to(owner_total.astype(jnp.bfloat16)[None, :], (owners, local))
    )
    back_send = jnp.concatenate([back_send, total_row], axis=1)
    back = lax.all_to_all(back_send, "expert", split_axis=0, concat_axis=0, tiled=True)
    total_load = back[:, local * capacity, :local].astype(jnp.float32).reshape(experts)
    back = back[:, : local * capacity].reshape(experts * capacity, feature_cols)
    picked = back[target].astype(jnp.float32)
    weighted = picked * combine_weight.reshape(-1)[:, None]
    mixed = jnp.sum(weighted.reshape(tok_rows, chosen, feature_cols), axis=1).astype(jnp.bfloat16)
    all_tokens = tok_rows * lax.axis_size("dp") * owners
    expert_load = total_load * (experts / all_tokens)
    return (mixed, expert_load)


def solution(mesh):
    in_specs = (
        P(("dp", "expert"), "tensor"),
        P(("dp", "expert"), None),
        P(("dp", "expert"), None),
        P("expert", None, "tensor"),
        P("expert", None, "tensor"),
        P("expert", "tensor", None),
    )
    out_specs = (P(("dp", "expert"), "tensor"), P())
    return jax.shard_map(
        on_device, mesh=mesh, in_specs=in_specs, out_specs=out_specs, check_vma=False
    )
```

```python
import jax
import jax.numpy as jnp
from jax import lax
from jax.sharding import PartitionSpec as P


def on_device(tokens, expert_ids, combine_weight, w_gate, w_up, w_down):
    owners = lax.axis_size("expert")
    local = w_gate.shape[0]
    experts = owners * local
    tok_rows, feature_cols = tokens.shape
    chosen = expert_ids.shape[1]
    capacity = min(tok_rows, (9 * tok_rows * chosen + 8 * experts - 1) // (8 * experts))
    flat_ids = expert_ids.reshape(-1)
    onehot = (flat_ids[:, None] == jnp.arange(experts, dtype=jnp.int32)[None, :]).astype(jnp.int32)
    ranks = jnp.sum((jnp.cumsum(onehot, axis=0) - onehot) * onehot, axis=1)
    target = flat_ids * capacity + ranks
    pair_count = flat_ids.shape[0]
    source = (
        jnp.full((experts * capacity,), -1, jnp.int32)
        .at[target]
        .set(jnp.arange(pair_count, dtype=jnp.int32) // chosen)
    )
    filled = (source >= 0)[:, None]
    safe = jnp.maximum(source, 0)
    outgoing = jnp.where(filled, tokens[safe], jnp.zeros((), jnp.bfloat16))
    outgoing = outgoing.reshape(owners, local, capacity, feature_cols)
    group_load = jnp.sum(onehot.astype(jnp.float32) * combine_weight.reshape(-1)[:, None], axis=0)
    load_row = jnp.zeros((owners, 1, feature_cols), jnp.bfloat16)
    load_row = load_row.at[:, 0, :local].set(group_load.reshape(owners, local).astype(jnp.bfloat16))

    send = jnp.concatenate(
        [outgoing.reshape(owners, local * capacity, feature_cols), load_row], axis=1
    )
    got = lax.all_to_all(send, "expert", split_axis=0, concat_axis=0, tiled=True)
    owner_part = jnp.sum(got[:, local * capacity, :local].astype(jnp.float32), axis=0)
    got = got[:, : local * capacity].reshape(owners, local, capacity, feature_cols)
    got = jnp.transpose(got, (1, 0, 2, 3)).reshape(local * owners * capacity, feature_cols)
    arrived = lax.all_gather(got, "tensor", axis=1, tiled=True)
    model_width = arrived.shape[1]
    rows = arrived.reshape(local, owners * capacity, model_width)
    gate = jnp.einsum("erd,edh->erh", rows, w_gate, preferred_element_type=jnp.float32)
    up = jnp.einsum("erd,edh->erh", rows, w_up, preferred_element_type=jnp.float32)
    hidden = (jax.nn.silu(gate) * up).astype(jnp.bfloat16)
    splits = lax.axis_size("tensor")
    w_cols = lax.all_to_all(
        w_down.reshape(local, w_down.shape[1], splits, feature_cols),
        "tensor",
        split_axis=2,
        concat_axis=1,
        tiled=True,
    ).reshape(local, w_down.shape[1] * splits, feature_cols)
    hidden_all = lax.all_gather(hidden, "tensor", axis=2, tiled=True)
    expert_out = jnp.einsum(
        "erh,ehd->erd", hidden_all, w_cols, preferred_element_type=jnp.float32
    ).astype(jnp.bfloat16)
    back_send = jnp.transpose(
        expert_out.reshape(local, owners, capacity, feature_cols), (1, 0, 2, 3)
    ).reshape(owners, local * capacity, feature_cols)
    owner_total = lax.psum(owner_part, "dp")
    total_row = jnp.zeros((owners, 1, feature_cols), jnp.bfloat16)
    total_row = total_row.at[:, 0, :local].set(
        jnp.broadcast_to(owner_total.astype(jnp.bfloat16)[None, :], (owners, local))
    )
    back_send = jnp.concatenate([back_send, total_row], axis=1)
    back = lax.all_to_all(back_send, "expert", split_axis=0, concat_axis=0, tiled=True)
    total_load = back[:, local * capacity, :local].astype(jnp.float32).reshape(experts)
    back = back[:, : local * capacity].reshape(experts * capacity, feature_cols)
    picked = back[target].astype(jnp.float32)
    weighted = picked * combine_weight.reshape(-1)[:, None]
    mixed = jnp.sum(weighted.reshape(tok_rows, chosen, feature_cols), axis=1).astype(jnp.bfloat16)
    all_tokens = tok_rows * lax.axis_size("dp") * owners
    expert_load = total_load * (experts / all_tokens)
    return (mixed, expert_load)


def solution(mesh):
    in_specs = (
        P(("dp", "expert"), "tensor"),
        P(("dp", "expert"), None),
        P(("dp", "expert"), None),
        P("expert", None, "tensor"),
        P("expert", None, "tensor"),
        P("expert", "tensor", None),
    )
    out_specs = (P(("dp", "expert"), "tensor"), P())
    return jax.shard_map(
        on_device, mesh=mesh, in_specs=in_specs, out_specs=out_specs, check_vma=False
    )
```

```python
import jax
import jax.numpy as jnp
from jax import lax
from jax.sharding import PartitionSpec as P


def on_device(tokens, expert_ids, combine_weight, w_gate, w_up, w_down):
    owners = lax.axis_size("expert")
    local = w_gate.shape[0]
    experts = owners * local
    tok_rows, feature_cols = tokens.shape
    chosen = expert_ids.shape[1]
    capacity = min(tok_rows, (9 * tok_rows * chosen + 8 * experts - 1) // (8 * experts))
    flat_ids = expert_ids.reshape(-1)
    onehot = (flat_ids[:, None] == jnp.arange(experts, dtype=jnp.int32)[None, :]).astype(jnp.int32)
    ranks = jnp.sum((jnp.cumsum(onehot, axis=0) - onehot) * onehot, axis=1)
    target = flat_ids * capacity + ranks
    pair_count = flat_ids.shape[0]
    source = (
        jnp.full((experts * capacity,), -1, jnp.int32)
        .at[target]
        .set(jnp.arange(pair_count, dtype=jnp.int32) // chosen)
    )
    filled = (source >= 0)[:, None]
    safe = jnp.maximum(source, 0)
    outgoing = jnp.where(filled, tokens[safe], jnp.zeros((), jnp.bfloat16))
    outgoing = outgoing.reshape(owners, local, capacity, feature_cols)
    group_load = jnp.sum(onehot.astype(jnp.float32) * combine_weight.reshape(-1)[:, None], axis=0)
    load_row = jnp.zeros((owners, 1, feature_cols), jnp.bfloat16)
    load_row = load_row.at[:, 0, :local].set(group_load.reshape(owners, local).astype(jnp.bfloat16))

    send = jnp.concatenate(
        [outgoing.reshape(owners, local * capacity, feature_cols), load_row], axis=1
    )
    got = lax.all_to_all(send, "expert", split_axis=0, concat_axis=0, tiled=True)
    owner_part = jnp.sum(got[:, local * capacity, :local].astype(jnp.float32), axis=0)
    got = got[:, : local * capacity].reshape(owners, local, capacity, feature_cols)
    got = jnp.transpose(got, (1, 0, 2, 3)).reshape(local * owners * capacity, feature_cols)
    splits = lax.axis_size("tensor")
    me = lax.axis_index("tensor")
    hid_block = w_down.shape[1]
    w_blocks = w_down.reshape(local, hid_block, splits, feature_cols)
    received = []
    for shift in range(splits):
        block = lax.dynamic_index_in_dim(w_blocks, (me + shift) % splits, axis=2, keepdims=False)
        if shift:
            block = lax.ppermute(
                block, "tensor", [(j, (j + shift) % splits) for j in range(splits)]
            )
        received.append(block)
    w_cols = jnp.stack(received, axis=1)
    got, w_cols = lax.optimization_barrier((got, w_cols))
    arrived = lax.all_gather(got, "tensor", axis=1, tiled=True)
    model_width = arrived.shape[1]
    rows = arrived.reshape(local, owners * capacity, model_width)
    gate = jnp.einsum("erd,edh->erh", rows, w_gate, preferred_element_type=jnp.float32)
    up = jnp.einsum("erd,edh->erh", rows, w_up, preferred_element_type=jnp.float32)
    hidden = (jax.nn.silu(gate) * up).astype(jnp.bfloat16)
    hidden_all = lax.all_gather(hidden, "tensor", axis=2, tiled=True)
    hidden_all = hidden_all.reshape(local, owners * capacity, splits, hid_block)
    order = (me - jnp.arange(splits, dtype=jnp.int32)) % splits
    hidden_all = jnp.take(hidden_all, order, axis=2)
    expert_out = jnp.einsum(
        "ersh,eshd->erd", hidden_all, w_cols, preferred_element_type=jnp.float32
    ).astype(jnp.bfloat16)
    back_send = jnp.transpose(
        expert_out.reshape(local, owners, capacity, feature_cols), (1, 0, 2, 3)
    ).reshape(owners, local * capacity, feature_cols)
    owner_total = lax.psum(owner_part, "dp")
    total_row = jnp.zeros((owners, 1, feature_cols), jnp.bfloat16)
    total_row = total_row.at[:, 0, :local].set(
        jnp.broadcast_to(owner_total.astype(jnp.bfloat16)[None, :], (owners, local))
    )
    back_send = jnp.concatenate([back_send, total_row], axis=1)
    back = lax.all_to_all(back_send, "expert", split_axis=0, concat_axis=0, tiled=True)
    total_load = back[:, local * capacity, :local].astype(jnp.float32).reshape(experts)
    back = back[:, : local * capacity].reshape(experts * capacity, feature_cols)
    picked = back[target].astype(jnp.float32)
    weighted = picked * combine_weight.reshape(-1)[:, None]
    mixed = jnp.sum(weighted.reshape(tok_rows, chosen, feature_cols), axis=1).astype(jnp.bfloat16)
    all_tokens = tok_rows * lax.axis_size("dp") * owners
    expert_load = total_load * (experts / all_tokens)
    return (mixed, expert_load)


def solution(mesh):
    in_specs = (
        P(("dp", "expert"), "tensor"),
        P(("dp", "expert"), None),
        P(("dp", "expert"), None),
        P("expert", None, "tensor"),
        P("expert", None, "tensor"),
        P("expert", "tensor", None),
    )
    out_specs = (P(("dp", "expert"), "tensor"), P())
    return jax.shard_map(
        on_device, mesh=mesh, in_specs=in_specs, out_specs=out_specs, check_vma=False
    )
```

```python
import jax
import jax.numpy as jnp
from jax import lax
from jax.sharding import PartitionSpec as P


def on_device(tokens, expert_ids, combine_weight, w_gate, w_up, w_down):
    owners = lax.axis_size("expert")
    local = w_gate.shape[0]
    experts = owners * local
    tok_rows, feature_cols = tokens.shape
    chosen = expert_ids.shape[1]
    capacity = min(tok_rows, (9 * tok_rows * chosen + 8 * experts - 1) // (8 * experts))
    flat_ids = expert_ids.reshape(-1)
    onehot = (flat_ids[:, None] == jnp.arange(experts, dtype=jnp.int32)[None, :]).astype(jnp.int32)
    ranks = jnp.sum((jnp.cumsum(onehot, axis=0) - onehot) * onehot, axis=1)
    target = flat_ids * capacity + ranks
    slot_ids = jnp.arange(experts * capacity, dtype=jnp.int32)
    slot_of_token = jnp.any(
        (target[None, :] == slot_ids[:, None]).reshape(experts * capacity, tok_rows, chosen), axis=2
    )
    outgoing = jnp.dot(
        slot_of_token.astype(jnp.bfloat16), tokens, preferred_element_type=jnp.float32
    ).astype(jnp.bfloat16)
    outgoing = outgoing.reshape(owners, local, capacity, feature_cols)
    group_load = jnp.sum(onehot.astype(jnp.float32) * combine_weight.reshape(-1)[:, None], axis=0)
    load_row = jnp.zeros((owners, 1, feature_cols), jnp.bfloat16)
    load_row = load_row.at[:, 0, :local].set(group_load.reshape(owners, local).astype(jnp.bfloat16))

    send = jnp.concatenate(
        [outgoing.reshape(owners, local * capacity, feature_cols), load_row], axis=1
    )
    got = lax.all_to_all(send, "expert", split_axis=0, concat_axis=0, tiled=True)
    owner_part = jnp.sum(got[:, local * capacity, :local].astype(jnp.float32), axis=0)
    got = got[:, : local * capacity].reshape(owners, local, capacity, feature_cols)
    got = jnp.transpose(got, (1, 0, 2, 3)).reshape(local * owners * capacity, feature_cols)
    arrived = lax.all_gather(got, "tensor", axis=1, tiled=True)
    model_width = arrived.shape[1]
    rows = arrived.reshape(local, owners * capacity, model_width)
    gate = jnp.einsum("erd,edh->erh", rows, w_gate, preferred_element_type=jnp.float32)
    up = jnp.einsum("erd,edh->erh", rows, w_up, preferred_element_type=jnp.float32)
    hidden = (jax.nn.silu(gate) * up).astype(jnp.bfloat16)
    down = jnp.einsum("erh,ehd->erd", hidden, w_down, preferred_element_type=jnp.float32).astype(
        jnp.bfloat16
    )
    summed = lax.psum_scatter(
        down.reshape(local * owners * capacity, model_width), "tensor", scatter_dimension=1, tiled=True
    )
    back_send = jnp.transpose(
        summed.reshape(local, owners, capacity, feature_cols), (1, 0, 2, 3)
    ).reshape(owners, local * capacity, feature_cols)
    owner_total = lax.psum(owner_part, "dp")
    total_row = jnp.zeros((owners, 1, feature_cols), jnp.bfloat16)
    total_row = total_row.at[:, 0, :local].set(
        jnp.broadcast_to(owner_total.astype(jnp.bfloat16)[None, :], (owners, local))
    )
    back_send = jnp.concatenate([back_send, total_row], axis=1)
    back = lax.all_to_all(back_send, "expert", split_axis=0, concat_axis=0, tiled=True)
    total_load = back[:, local * capacity, :local].astype(jnp.float32).reshape(experts)
    back = back[:, : local * capacity].reshape(experts * capacity, feature_cols)
    weight_of_slot = jnp.sum(
        jnp.where(
            target[:, None] == slot_ids[None, :], combine_weight.reshape(-1)[:, None], 0.0
        ).reshape(tok_rows, chosen, experts * capacity),
        axis=1,
    )
    mixed = jnp.dot(
        weight_of_slot,
        back.astype(jnp.float32),
        precision=lax.Precision.HIGHEST,
        preferred_element_type=jnp.float32,
    ).astype(jnp.bfloat16)
    all_tokens = tok_rows * lax.axis_size("dp") * owners
    expert_load = total_load * (experts / all_tokens)
    return (mixed, expert_load)


def solution(mesh):
    in_specs = (
        P(("dp", "expert"), "tensor"),
        P(("dp", "expert"), None),
        P(("dp", "expert"), None),
        P("expert", None, "tensor"),
        P("expert", None, "tensor"),
        P("expert", "tensor", None),
    )
    out_specs = (P(("dp", "expert"), "tensor"), P())
    return jax.shard_map(
        on_device, mesh=mesh, in_specs=in_specs, out_specs=out_specs, check_vma=False
    )
```

```python
import jax
import jax.numpy as jnp
from jax import lax
from jax.sharding import PartitionSpec as P


def on_device(tokens, expert_ids, combine_weight, w_gate, w_up, w_down):
    owners = lax.axis_size("expert")
    local = w_gate.shape[0]
    experts = owners * local
    tok_rows, feature_cols = tokens.shape
    chosen = expert_ids.shape[1]
    capacity = min(tok_rows, (9 * tok_rows * chosen + 8 * experts - 1) // (8 * experts))
    flat_ids = expert_ids.reshape(-1)
    onehot = (flat_ids[:, None] == jnp.arange(experts, dtype=jnp.int32)[None, :]).astype(jnp.int32)
    ranks = jnp.sum((jnp.cumsum(onehot, axis=0) - onehot) * onehot, axis=1)
    target = flat_ids * capacity + ranks
    slot_ids = jnp.arange(experts * capacity, dtype=jnp.int32)
    slot_of_token = jnp.any(
        (target[None, :] == slot_ids[:, None]).reshape(experts * capacity, tok_rows, chosen), axis=2
    )
    outgoing = jnp.dot(
        slot_of_token.astype(jnp.bfloat16), tokens, preferred_element_type=jnp.float32
    ).astype(jnp.bfloat16)
    outgoing = outgoing.reshape(owners, local, capacity, feature_cols)
    group_load = jnp.sum(onehot.astype(jnp.float32) * combine_weight.reshape(-1)[:, None], axis=0)
    load_row = jnp.zeros((owners, 1, feature_cols), jnp.bfloat16)
    load_row = load_row.at[:, 0, :local].set(group_load.reshape(owners, local).astype(jnp.bfloat16))

    send = jnp.concatenate(
        [outgoing.reshape(owners, local * capacity, feature_cols), load_row], axis=1
    )
    got = lax.all_to_all(
        send.reshape(owners, -1, 128), "expert", split_axis=0, concat_axis=0, tiled=True
    ).reshape(send.shape)
    owner_part = jnp.sum(got[:, local * capacity, :local].astype(jnp.float32), axis=0)
    got = got[:, : local * capacity].reshape(owners, local, capacity, feature_cols)
    got = jnp.transpose(got, (1, 0, 2, 3)).reshape(local * owners * capacity, feature_cols)
    arrived = lax.all_gather(got, "tensor", axis=1, tiled=True)
    model_width = arrived.shape[1]
    rows = arrived.reshape(local, owners * capacity, model_width)
    gate = jnp.einsum("erd,edh->erh", rows, w_gate, preferred_element_type=jnp.float32)
    up = jnp.einsum("erd,edh->erh", rows, w_up, preferred_element_type=jnp.float32)
    hidden = (jax.nn.silu(gate) * up).astype(jnp.bfloat16)
    down = jnp.einsum("erh,ehd->erd", hidden, w_down, preferred_element_type=jnp.float32).astype(
        jnp.bfloat16
    )
    summed = lax.psum_scatter(
        down.reshape(local * owners * capacity, model_width), "tensor", scatter_dimension=1, tiled=True
    )
    back_send = jnp.transpose(
        summed.reshape(local, owners, capacity, feature_cols), (1, 0, 2, 3)
    ).reshape(owners, local * capacity, feature_cols)
    owner_total = lax.psum(owner_part, "dp")
    total_row = jnp.zeros((owners, 1, feature_cols), jnp.bfloat16)
    total_row = total_row.at[:, 0, :local].set(
        jnp.broadcast_to(owner_total.astype(jnp.bfloat16)[None, :], (owners, local))
    )
    back_send = jnp.concatenate([back_send, total_row], axis=1)
    back = lax.all_to_all(
        back_send.reshape(owners, -1, 128), "expert", split_axis=0, concat_axis=0, tiled=True
    ).reshape(back_send.shape)
    total_load = back[:, local * capacity, :local].astype(jnp.float32).reshape(experts)
    back = back[:, : local * capacity].reshape(experts * capacity, feature_cols)
    weight_of_slot = jnp.sum(
        jnp.where(
            target[:, None] == slot_ids[None, :], combine_weight.reshape(-1)[:, None], 0.0
        ).reshape(tok_rows, chosen, experts * capacity),
        axis=1,
    )
    mixed = jnp.dot(
        weight_of_slot,
        back.astype(jnp.float32),
        precision=lax.Precision.HIGHEST,
        preferred_element_type=jnp.float32,
    ).astype(jnp.bfloat16)
    all_tokens = tok_rows * lax.axis_size("dp") * owners
    expert_load = total_load * (experts / all_tokens)
    return (mixed, expert_load)


def solution(mesh):
    in_specs = (
        P(("dp", "expert"), "tensor"),
        P(("dp", "expert"), None),
        P(("dp", "expert"), None),
        P("expert", None, "tensor"),
        P("expert", None, "tensor"),
        P("expert", "tensor", None),
    )
    out_specs = (P(("dp", "expert"), "tensor"), P())
    return jax.shard_map(
        on_device, mesh=mesh, in_specs=in_specs, out_specs=out_specs, check_vma=False
    )
```

```python
import jax
import jax.numpy as jnp
from jax import lax
from jax.sharding import PartitionSpec as P


def on_device(tokens, expert_ids, combine_weight, w_gate, w_up, w_down):
    owners = lax.axis_size("expert")
    local = w_gate.shape[0]
    experts = owners * local
    tok_rows, feature_cols = tokens.shape
    chosen = expert_ids.shape[1]
    capacity = min(tok_rows, (9 * tok_rows * chosen + 8 * experts - 1) // (8 * experts))
    flat_ids = expert_ids.reshape(-1)
    onehot = (flat_ids[:, None] == jnp.arange(experts, dtype=jnp.int32)[None, :]).astype(jnp.int32)
    ranks = jnp.sum((jnp.cumsum(onehot, axis=0) - onehot) * onehot, axis=1)
    target = flat_ids * capacity + ranks
    slot_ids = jnp.arange(experts * capacity, dtype=jnp.int32)
    slot_of_token = jnp.any(
        (target[None, :] == slot_ids[:, None]).reshape(experts * capacity, tok_rows, chosen), axis=2
    )
    outgoing = jnp.dot(
        slot_of_token.astype(jnp.bfloat16), tokens, preferred_element_type=jnp.float32
    ).astype(jnp.bfloat16)
    outgoing = outgoing.reshape(owners, local, capacity, feature_cols)
    group_load = jnp.sum(onehot.astype(jnp.float32) * combine_weight.reshape(-1)[:, None], axis=0)
    lanes = 128
    per_row = feature_cols // lanes
    data_rows = local * capacity * per_row
    load_row = jnp.zeros((owners, per_row, lanes), jnp.bfloat16)
    load_row = load_row.at[:, 0, :local].set(group_load.reshape(owners, local).astype(jnp.bfloat16))

    send = jnp.concatenate([outgoing.reshape(owners, data_rows, lanes), load_row], axis=1)
    got = lax.all_to_all(send, "expert", split_axis=0, concat_axis=0, tiled=True)
    owner_part = jnp.sum(got[:, data_rows, :local].astype(jnp.float32), axis=0)
    got = got[:, :data_rows].reshape(owners, local, capacity * per_row, lanes)
    got = jnp.transpose(got, (1, 0, 2, 3)).reshape(local * owners * capacity, feature_cols)
    arrived = lax.all_gather(got, "tensor", axis=1, tiled=True)
    model_width = arrived.shape[1]
    rows = arrived.reshape(local, owners * capacity, model_width)
    gate = jnp.einsum("erd,edh->erh", rows, w_gate, preferred_element_type=jnp.float32)
    up = jnp.einsum("erd,edh->erh", rows, w_up, preferred_element_type=jnp.float32)
    hidden = (jax.nn.silu(gate) * up).astype(jnp.bfloat16)
    down = jnp.einsum("erh,ehd->erd", hidden, w_down, preferred_element_type=jnp.float32).astype(
        jnp.bfloat16
    )
    summed = lax.psum_scatter(
        down.reshape(local * owners * capacity, model_width), "tensor", scatter_dimension=1, tiled=True
    )
    back_send = jnp.transpose(
        summed.reshape(local, owners, capacity * per_row, lanes), (1, 0, 2, 3)
    ).reshape(owners, data_rows, lanes)
    owner_total = lax.psum(owner_part, "dp")
    total_row = jnp.zeros((owners, per_row, lanes), jnp.bfloat16)
    total_row = total_row.at[:, 0, :local].set(
        jnp.broadcast_to(owner_total.astype(jnp.bfloat16)[None, :], (owners, local))
    )
    back_send = jnp.concatenate([back_send, total_row], axis=1)
    back = lax.all_to_all(back_send, "expert", split_axis=0, concat_axis=0, tiled=True)
    total_load = back[:, data_rows, :local].astype(jnp.float32).reshape(experts)
    back = back[:, :data_rows].reshape(experts * capacity, feature_cols)
    weight_of_slot = jnp.sum(
        jnp.where(
            target[:, None] == slot_ids[None, :], combine_weight.reshape(-1)[:, None], 0.0
        ).reshape(tok_rows, chosen, experts * capacity),
        axis=1,
    )
    mixed = jnp.dot(
        weight_of_slot,
        back.astype(jnp.float32),
        precision=lax.Precision.HIGHEST,
        preferred_element_type=jnp.float32,
    ).astype(jnp.bfloat16)
    all_tokens = tok_rows * lax.axis_size("dp") * owners
    expert_load = total_load * (experts / all_tokens)
    return (mixed, expert_load)


def solution(mesh):
    in_specs = (
        P(("dp", "expert"), "tensor"),
        P(("dp", "expert"), None),
        P(("dp", "expert"), None),
        P("expert", None, "tensor"),
        P("expert", None, "tensor"),
        P("expert", "tensor", None),
    )
    out_specs = (P(("dp", "expert"), "tensor"), P())
    return jax.shard_map(
        on_device, mesh=mesh, in_specs=in_specs, out_specs=out_specs, check_vma=False
    )
```

```python
import jax
import jax.numpy as jnp
from jax import lax
from jax.sharding import PartitionSpec as P


def on_device(tokens, expert_ids, combine_weight, w_gate, w_up, w_down):
    owners = lax.axis_size("expert")
    local = w_gate.shape[0]
    experts = owners * local
    tok_rows, feature_cols = tokens.shape
    chosen = expert_ids.shape[1]
    capacity = min(tok_rows, (9 * tok_rows * chosen + 8 * experts - 1) // (8 * experts))
    flat_ids = expert_ids.reshape(-1)
    onehot = (flat_ids[:, None] == jnp.arange(experts, dtype=jnp.int32)[None, :]).astype(jnp.int32)
    ranks = jnp.sum((jnp.cumsum(onehot, axis=0) - onehot) * onehot, axis=1)
    target = flat_ids * capacity + ranks
    slot_ids = jnp.arange(experts * capacity, dtype=jnp.int32)
    slot_of_token = jnp.any(
        (target[None, :] == slot_ids[:, None]).reshape(experts * capacity, tok_rows, chosen), axis=2
    )
    outgoing = jnp.dot(
        slot_of_token.astype(jnp.bfloat16), tokens, preferred_element_type=jnp.float32
    ).astype(jnp.bfloat16)
    outgoing = outgoing.reshape(owners, local, capacity, feature_cols)
    group_load = jnp.sum(onehot.astype(jnp.float32) * combine_weight.reshape(-1)[:, None], axis=0)
    lanes = 128
    per_row = feature_cols // lanes
    data_rows = local * capacity * per_row
    load_row = jnp.zeros((owners, per_row, lanes), jnp.bfloat16)
    load_row = load_row.at[:, 0, :local].set(group_load.reshape(owners, local).astype(jnp.bfloat16))

    send = jnp.concatenate([outgoing.reshape(owners, data_rows, lanes), load_row], axis=1)
    got = lax.all_to_all(send, "expert", split_axis=0, concat_axis=0, tiled=True)
    owner_part = jnp.sum(got[:, data_rows, :local].astype(jnp.float32), axis=0)
    got = got[:, :data_rows].reshape(owners, local, capacity * per_row, lanes)
    got = jnp.transpose(got, (1, 0, 2, 3)).reshape(local * owners * capacity, feature_cols)
    arrived = lax.all_gather(got, "tensor", axis=1, tiled=True)
    model_width = arrived.shape[1]
    rows = arrived.reshape(local, owners * capacity, model_width)
    gate = jnp.einsum("erd,edh->erh", rows, w_gate, preferred_element_type=jnp.float32)
    up = jnp.einsum("erd,edh->erh", rows, w_up, preferred_element_type=jnp.float32)
    hidden = (jax.nn.silu(gate) * up).astype(jnp.bfloat16)
    down = jnp.einsum("erh,ehd->erd", hidden, w_down, preferred_element_type=jnp.float32).astype(
        jnp.bfloat16
    )
    summed = lax.psum_scatter(
        down.reshape(local * owners * capacity, model_width), "tensor", scatter_dimension=1, tiled=True
    )
    back_send = jnp.transpose(
        summed.reshape(local, owners, capacity * per_row, lanes), (1, 0, 2, 3)
    ).reshape(owners, data_rows, lanes)
    owner_total = lax.psum(owner_part, "dp")
    total_row = jnp.zeros((owners, per_row, lanes), jnp.bfloat16)
    total_row = total_row.at[:, 0, :local].set(
        jnp.broadcast_to(owner_total.astype(jnp.bfloat16)[None, :], (owners, local))
    )
    back_send = jnp.concatenate([back_send, total_row], axis=1)
    back = lax.all_to_all(back_send, "expert", split_axis=0, concat_axis=0, tiled=True)
    total_load = back[:, data_rows, :local].astype(jnp.float32).reshape(experts)
    weight_of_slot = jnp.sum(
        jnp.where(
            target[:, None] == slot_ids[None, :], combine_weight.reshape(-1)[:, None], 0.0
        ).reshape(tok_rows, chosen, experts * capacity),
        axis=1,
    )
    lane_group = jnp.arange(per_row, dtype=jnp.int32)
    spread = jnp.where(
        lane_group[:, None, None, None, None] == lane_group[None, None, None, None, :],
        weight_of_slot.reshape(1, tok_rows, owners, local * capacity, 1),
        0.0,
    ).reshape(per_row, tok_rows, owners, data_rows)
    spread = jnp.pad(spread, ((0, 0), (0, 0), (0, 0), (0, back.shape[1] - data_rows)))
    mixed = jnp.einsum(
        "qtoj,ojl->tql",
        spread,
        back.astype(jnp.float32),
        precision=lax.Precision.HIGHEST,
        preferred_element_type=jnp.float32,
    ).reshape(tok_rows, feature_cols).astype(jnp.bfloat16)
    all_tokens = tok_rows * lax.axis_size("dp") * owners
    expert_load = total_load * (experts / all_tokens)
    return (mixed, expert_load)


def solution(mesh):
    in_specs = (
        P(("dp", "expert"), "tensor"),
        P(("dp", "expert"), None),
        P(("dp", "expert"), None),
        P("expert", None, "tensor"),
        P("expert", None, "tensor"),
        P("expert", "tensor", None),
    )
    out_specs = (P(("dp", "expert"), "tensor"), P())
    return jax.shard_map(
        on_device, mesh=mesh, in_specs=in_specs, out_specs=out_specs, check_vma=False
    )
```
